128 devices in a mesh: section: 64 (over z, y, x), expert: 2 (over core).
Axes of the slice: x: 4, y: 4, z: 4, core: 2. Of those that a mesh axis runs over, the one named last changes fastest.
Arguments:
- state: bfloat16 [64, 2048, 3584], P('section', 'expert'), may hold values from -6 to 6
- norm_gain: float32 [64, 3584], P('section'), may hold values from 0.1 to 1.9
- router: bfloat16 [64, 3584, 128], P('section'), may hold values from -0.1875 to 0.1875
- w_gate: bfloat16 [64, 3584, 1024], P('section', None, 'expert'), may hold values from -0.09375 to 0.09375
- w_up: bfloat16 [64, 3584, 1024], P('section', None, 'expert'), may hold values from -0.09375 to 0.09375
- w_down: bfloat16 [64, 1024, 3584], P('section', 'expert'), may hold values from -0.25 to 0.25
- route_ids: int32 [1, 64, 2048, 8], P(None, 'section', 'expert'), may hold values from 0 to 127, as said below
Outputs:
- state_out: bfloat16 [64, 2048, 3584], P('section', 'expert')
The draws below stay inside these ranges and needn't reach their ends.
Inputs may be any that keep to these rules, and one draw needn't show every extreme that they name: `route_ids`: each row names 8 different experts; expert 0 is the expert whose weights are given.
All inputs are finite; a program needn't handle non-finite values.
Results may differ from the reference program's by a relative error of at most 0.002.
Values may be sent and summed in bfloat16 or wider, within the bound.
No kernel may reach another device: no remote copies, remote signals or barrier semaphores. Data moves between devices by JAX's collectives and lax.ppermute only.
A program may use at most 128 MiB of HBM per device.

```python
import jax
import jax.numpy as jnp
from jax import lax

D = 3584
HE_DEV = 512
EXPERTS = 128
TOP = 8
TICKS = 1
TOK_DEV = 1024
CAP = 128
EXPERT_HID = 1024
MB_TOK = 2048
LAYERS = 64
N_EXPERT = 2


def draw_route_ids(key, part):
    keys = jax.random.split(key, 5)
    rows_shape = (TICKS, LAYERS, MB_TOK)
    level = jax.random.randint(keys[0], (TICKS, LAYERS, MB_TOK // TOK_DEV), 1, 5)
    level_rows = jnp.repeat(level, TOK_DEV, axis=2)
    coin = jax.random.randint(keys[1], rows_shape, 0, 16)
    chosen = coin < level_rows
    base = jax.random.randint(keys[2], rows_shape, 0, EXPERTS - 1)
    stride = jax.random.randint(keys[3], rows_shape, 1, (EXPERTS - 2) // 7 + 1)
    position = jax.random.randint(keys[4], rows_shape, 0, TOP)
    order = jnp.arange(TOP).astype(jnp.int32)
    ids = 1 + (base[..., None] + order * stride[..., None]) % (EXPERTS - 1)
    ids = jnp.where(chosen[..., None] & (order == position[..., None]), 0, ids)
    return ids.astype(jnp.int32)


def block_scale(own_key, dims, cuts, low, top_value):
    level, own = 1.0, jax.random.fold_in(own_key, 6)
    for dim, parts in cuts:
        steps = jnp.exp(jax.random.uniform(jax.random.fold_in(own, dim), (parts,), jnp.float32, low / len(cuts), top_value / len(cuts)))
        level = level * jnp.repeat(steps, dims[dim] // parts).reshape([-1 if axis == dim else 1 for axis in range(len(dims))])
    return level


def noise(rng, dims, spread, reach, pieces=(), held_as=jnp.bfloat16):
    drawn = spread * jax.random.normal(rng, dims, jnp.float32)
    if pieces:
        drawn = drawn * block_scale(rng, dims, pieces, -0.22, 0.18)
    return jnp.clip(drawn, -reach, reach).astype(held_as)


def setup_inputs(seed: int = 0) -> dict:
    streams_of = jax.random.split(jax.random.key(seed), 8)
    state = noise(streams_of[0], (LAYERS, MB_TOK, D), 1.0, 6.0, ((0, 64), (1, 2)))
    norm_gain = jnp.clip(1.0 + 0.18 * jax.random.normal(streams_of[1], (LAYERS, D), jnp.float32), 0.1, 1.9)
    router = noise(streams_of[2], (LAYERS, D, EXPERTS), (D // 4) ** -0.5, 0.1875, ((0, 64),))
    w_gate = noise(streams_of[3], (LAYERS, D, EXPERT_HID), D ** -0.5, 0.09375, ((0, 64), (2, 2)))
    w_up = noise(streams_of[4], (LAYERS, D, EXPERT_HID), D ** -0.5, 0.09375, ((0, 64), (2, 2)))
    w_down = noise(streams_of[5], (LAYERS, EXPERT_HID, D), HE_DEV ** -0.5, 0.25, ((0, 64), (1, 2)))
    route_ids = draw_route_ids(jax.random.fold_in(streams_of[7], 71), 0)
    return dict(state=state, norm_gain=norm_gain, router=router, w_gate=w_gate, w_up=w_up, w_down=w_down, route_ids=route_ids)


def segment_step(args):
    h, gain, router, w_gate, w_up, w_down, ids = args
    h32 = h.astype(jnp.float32)
    var = lax.optimization_barrier(jnp.mean(h32 * h32, axis=-1, keepdims=True))
    normed = (h32 * lax.rsqrt(var + 1e-06) * gain).astype(jnp.bfloat16)
    scores = jax.nn.sigmoid(jnp.dot(normed, router, preferred_element_type=jnp.float32))
    expert_iota = jnp.arange(EXPERTS).astype(jnp.int32)
    picked = lax.optimization_barrier(jnp.sum((ids[:, :, None] == expert_iota[None, None, :]).astype(jnp.float32), axis=1))
    weight = 2.5 * scores[:, 0] * picked[:, 0] / lax.optimization_barrier(jnp.sum(scores * picked, axis=-1))
    chosen = lax.optimization_barrier(jnp.sum((ids == 0).astype(jnp.int32), axis=-1)).reshape(N_EXPERT, TOK_DEV)
    slot = jnp.cumsum(chosen, axis=-1).astype(jnp.int32) - chosen
    kept = (chosen > 0) & (slot < CAP)
    slot_iota = jnp.arange(CAP).astype(jnp.int32)
    onehot = (kept[:, None, :] & (slot[:, None, :] == slot_iota[None, :, None])).astype(jnp.float32)
    blocks = normed.astype(jnp.float32).reshape(N_EXPERT, TOK_DEV, D)
    packed = jnp.einsum('bjt,btd->bjd', onehot, blocks, precision=lax.Precision.HIGHEST)
    packed = packed.astype(jnp.bfloat16).reshape(N_EXPERT * CAP, D)
    gate = jnp.dot(packed, w_gate, preferred_element_type=jnp.float32)
    upper = jnp.dot(packed, w_up, preferred_element_type=jnp.float32)
    active = (jax.nn.silu(gate) * upper).astype(jnp.bfloat16)
    expert_out = jnp.zeros((N_EXPERT * CAP, D), jnp.float32)
    for block in range(N_EXPERT):
        part = jnp.dot(active[:, block * HE_DEV:(block + 1) * HE_DEV], w_down[block * HE_DEV:(block + 1) * HE_DEV], preferred_element_type=jnp.float32)
        part = lax.optimization_barrier(part.astype(jnp.bfloat16)).astype(jnp.float32)
        expert_out = expert_out + part
    share = jnp.einsum('bjt,bt->bj', onehot, weight.reshape(N_EXPERT, TOK_DEV), precision=lax.Precision.HIGHEST)
    scaled = expert_out.reshape(N_EXPERT, CAP, D) * share[:, :, None]
    delta = jnp.einsum('bjt,bjd->btd', onehot, scaled, precision=lax.Precision.HIGHEST).reshape(N_EXPERT * TOK_DEV, D)
    return (h32 + delta).astype(jnp.bfloat16)

def reference(state, norm_gain, router, w_gate, w_up, w_down, route_ids):
    current = state
    for tick in range(TICKS):
        current = lax.map(segment_step, (current, norm_gain, router, w_gate, w_up, w_down, route_ids[tick]))
        current = jnp.roll(current, 1, axis=0)
    return current
```

```python
import jax
import jax.numpy as jnp
from jax import lax
from jax.sharding import PartitionSpec as P


def passed_along(x, axis, by):
    devices = lax.axis_size(axis)
    return lax.ppermute(x, axis, [(i, (i + by) % devices) for i in range(devices)])


def swapped(x, axis):
    return lax.ppermute(x, axis, [(0, 1), (1, 0)])


def expert_part(piece, gate_dev, up_dev, down_dev):
    gate = jnp.dot(piece, gate_dev, preferred_element_type=jnp.float32)
    upper = jnp.dot(piece, up_dev, preferred_element_type=jnp.float32)
    active = (jax.nn.silu(gate) * upper).astype(jnp.bfloat16)
    partial_out = jnp.dot(active, down_dev, preferred_element_type=jnp.float32)
    return lax.optimization_barrier(partial_out.astype(jnp.bfloat16))


def local(state, norm_gain, router, w_gate, w_up, w_down, route_ids):
    gate_dev = w_gate[0]
    up_dev = w_up[0]
    down_dev = w_down[0]
    gain = norm_gain[0]
    table = router[0]
    current = state[0]
    moved = passed_along(current, "section", 1)
    rows = current.shape[0]
    capacity = rows // 8
    me = lax.axis_index("expert")
    slot_iota = jnp.arange(capacity)[:, None]
    expert_iota = jnp.arange(table.shape[1])
    h32 = current.astype(jnp.float32)
    var = jnp.mean(h32 * h32, axis=-1, keepdims=True)
    normed = (h32 * lax.rsqrt(var + 1e-06) * gain).astype(jnp.bfloat16)
    scores = jax.nn.sigmoid(jnp.dot(normed, table, preferred_element_type=jnp.float32))
    ids = route_ids[0, 0]
    picked = jnp.sum((ids[:, :, None] == expert_iota[None, None, :]).astype(jnp.float32), axis=1)
    weight = 2.5 * scores[:, 0] * picked[:, 0] / jnp.sum(scores * picked, axis=-1)
    chosen = jnp.sum((ids == 0).astype(jnp.int32), axis=-1)
    slot = jnp.cumsum(chosen) - chosen
    kept = (chosen > 0) & (slot < capacity)
    hit = kept[None, :] & (slot[None, :] == slot_iota)
    onehot = hit.astype(jnp.bfloat16)
    row_iota = jnp.arange(rows, dtype=jnp.int32)
    row_of_slot = jnp.sum(jnp.where(hit, row_iota[None, :], 0), axis=1)
    row_of_slot = jnp.where(jnp.any(hit, axis=1), row_of_slot, rows)
    packed = jnp.dot(onehot, normed, preferred_element_type=jnp.float32).astype(jnp.bfloat16)
    other = swapped(packed, "expert")
    both = jnp.where(me == 0, jnp.concatenate([packed, other], axis=0),
                     jnp.concatenate([other, packed], axis=0))
    partials = expert_part(both, gate_dev, up_dev, down_dev)
    mine = jnp.where(me == 0, partials[:capacity], partials[capacity:])
    theirs = jnp.where(me == 0, partials[capacity:], partials[:capacity])
    summed = mine.astype(jnp.float32) + swapped(theirs, "expert").astype(jnp.float32)
    share = jnp.dot(onehot.astype(jnp.float32), weight, precision=lax.Precision.HIGHEST)
    scaled = summed * share[:, None]
    h_rows = jnp.dot(onehot, current, preferred_element_type=jnp.float32)
    new_rows = (h_rows + scaled).astype(jnp.bfloat16)
    new_rows = passed_along(new_rows, "section", 1)
    where_rows = passed_along(row_of_slot, "section", 1)
    out = moved.at[where_rows].set(new_rows, mode="drop", unique_indices=True)
    return out[None]


def solution(mesh):
    return jax.shard_map(
        local,
        mesh=mesh,
        in_specs=(
            P("section", "expert", None),
            P("section", None),
            P("section", None, None),
            P("section", None, "expert"),
            P("section", None, "expert"),
            P("section", "expert", None),
            P(None, "section", "expert", None),
        ),
        out_specs=P("section", "expert", None),
        check_vma=False,
    )
```

```python
import jax
import jax.numpy as jnp
from jax import lax
from jax.sharding import PartitionSpec as P

DIRECT_ROWS = 752


def passed_along(x, axis, by):
    devices = lax.axis_size(axis)
    return lax.ppermute(x, axis, [(i, (i + by) % devices) for i in range(devices)])


def x_minus(s, row=4):
    x = s % row
    return s - x + (x - 1) % row


def around(x, axis):
    devices = lax.axis_size(axis)
    step = [(i, x_minus(i)) for i in range(devices)]
    x = lax.ppermute(x, axis, step)
    x = lax.ppermute(x, axis, step)
    last = [(x_minus(x_minus(i)), (i + 1) % devices) for i in range(devices)]
    return lax.ppermute(x, axis, last)


def swapped(x, axis):
    return lax.ppermute(x, axis, [(0, 1), (1, 0)])


def expert_part(piece, gate_dev, up_dev, down_dev):
    gate = jnp.dot(piece, gate_dev, preferred_element_type=jnp.float32)
    upper = jnp.dot(piece, up_dev, preferred_element_type=jnp.float32)
    active = (jax.nn.silu(gate) * upper).astype(jnp.bfloat16)
    partial_out = jnp.dot(active, down_dev, preferred_element_type=jnp.float32)
    return lax.optimization_barrier(partial_out.astype(jnp.bfloat16))


def local(state, norm_gain, router, w_gate, w_up, w_down, route_ids):
    gate_dev = w_gate[0]
    up_dev = w_up[0]
    down_dev = w_down[0]
    gain = norm_gain[0]
    table = router[0]
    current = state[0]
    split = DIRECT_ROWS
    moved_near = passed_along(current[:split], "section", 1)
    moved_far = around(current[split:], "section")
    rows = current.shape[0]
    capacity = rows // 8
    me = lax.axis_index("expert")
    slot_iota = jnp.arange(capacity)[:, None]
    expert_iota = jnp.arange(table.shape[1])
    h32 = current.astype(jnp.float32)
    var = jnp.mean(h32 * h32, axis=-1, keepdims=True)
    normed = (h32 * lax.rsqrt(var + 1e-06) * gain).astype(jnp.bfloat16)
    scores = jax.nn.sigmoid(jnp.dot(normed, table, preferred_element_type=jnp.float32))
    ids = route_ids[0, 0]
    picked = jnp.sum((ids[:, :, None] == expert_iota[None, None, :]).astype(jnp.float32), axis=1)
    weight = 2.5 * scores[:, 0] * picked[:, 0] / jnp.sum(scores * picked, axis=-1)
    chosen = jnp.sum((ids == 0).astype(jnp.int32), axis=-1)
    slot = jnp.cumsum(chosen) - chosen
    kept = (chosen > 0) & (slot < capacity)
    hit = kept[None, :] & (slot[None, :] == slot_iota)
    onehot = hit.astype(jnp.bfloat16)
    row_iota = jnp.arange(rows, dtype=jnp.int32)
    row_of_slot = jnp.sum(jnp.where(hit, row_iota[None, :], 0), axis=1)
    row_of_slot = jnp.where(jnp.any(hit, axis=1), row_of_slot, rows)
    packed = jnp.dot(onehot, normed, preferred_element_type=jnp.float32).astype(jnp.bfloat16)
    other = swapped(packed, "expert")
    both = jnp.where(me == 0, jnp.concatenate([packed, other], axis=0),
                     jnp.concatenate([other, packed], axis=0))
    partials = expert_part(both, gate_dev, up_dev, down_dev)
    mine = jnp.where(me == 0, partials[:capacity], partials[capacity:])
    theirs = jnp.where(me == 0, partials[capacity:], partials[:capacity])
    summed = mine.astype(jnp.float32) + swapped(theirs, "expert").astype(jnp.float32)
    share = jnp.dot(onehot.astype(jnp.float32), weight, precision=lax.Precision.HIGHEST)
    scaled = summed * share[:, None]
    h_rows = jnp.dot(onehot, current, preferred_element_type=jnp.float32)
    new_rows = (h_rows + scaled).astype(jnp.bfloat16)
    new_rows = passed_along(new_rows, "section", 1)
    where_rows = passed_along(row_of_slot, "section", 1)
    moved = jnp.concatenate([moved_near, moved_far], axis=0)
    out = moved.at[where_rows].set(new_rows, mode="drop", unique_indices=True)
    return out[None]


def solution(mesh):
    return jax.shard_map(
        local,
        mesh=mesh,
        in_specs=(
            P("section", "expert", None),
            P("section", None),
            P("section", None, None),
            P("section", None, "expert"),
            P("section", None, "expert"),
            P("section", "expert", None),
            P(None, "section", "expert", None),
        ),
        out_specs=P("section", "expert", None),
        check_vma=False,
    )
```

```python
import jax
import jax.numpy as jnp
from jax import lax
from jax.sharding import PartitionSpec as P

DIRECT_ROWS = 816


def passed_along(x, axis, by):
    devices = lax.axis_size(axis)
    return lax.ppermute(x, axis, [(i, (i + by) % devices) for i in range(devices)])


def x_minus(s, row=4):
    x = s % row
    return s - x + (x - 1) % row


def around(x, axis):
    devices = lax.axis_size(axis)
    step = [(i, x_minus(i)) for i in range(devices)]
    x = lax.ppermute(x, axis, step)
    x = lax.ppermute(x, axis, step)
    last = [(x_minus(x_minus(i)), (i + 1) % devices) for i in range(devices)]
    return lax.ppermute(x, axis, last)


def swapped(x, axis):
    return lax.ppermute(x, axis, [(0, 1), (1, 0)])


def expert_part(piece, gate_dev, up_dev, down_dev):
    gate = jnp.dot(piece, gate_dev, preferred_element_type=jnp.float32)
    upper = jnp.dot(piece, up_dev, preferred_element_type=jnp.float32)
    active = (jax.nn.silu(gate) * upper).astype(jnp.bfloat16)
    partial_out = jnp.dot(active, down_dev, preferred_element_type=jnp.float32)
    return lax.optimization_barrier(partial_out.astype(jnp.bfloat16))


def local(state, norm_gain, router, w_gate, w_up, w_down, route_ids):
    gate_dev = w_gate[0]
    up_dev = w_up[0]
    down_dev = w_down[0]
    gain = norm_gain[0]
    table = router[0]
    current = state[0]
    split = DIRECT_ROWS
    moved_near = passed_along(current[:split], "section", 1)
    moved_far = around(current[split:], "section")
    rows = current.shape[0]
    capacity = rows // 8
    me = lax.axis_index("expert")
    slot_iota = jnp.arange(capacity)[:, None]
    expert_iota = jnp.arange(table.shape[1])
    h32 = current.astype(jnp.float32)
    var = jnp.mean(h32 * h32, axis=-1, keepdims=True)
    normed = (h32 * lax.rsqrt(var + 1e-06) * gain).astype(jnp.bfloat16)
    scores = jax.nn.sigmoid(jnp.dot(normed, table, preferred_element_type=jnp.float32))
    ids = route_ids[0, 0]
    picked = jnp.sum((ids[:, :, None] == expert_iota[None, None, :]).astype(jnp.float32), axis=1)
    weight = 2.5 * scores[:, 0] * picked[:, 0] / jnp.sum(scores * picked, axis=-1)
    chosen = jnp.sum((ids == 0).astype(jnp.int32), axis=-1)
    slot = jnp.cumsum(chosen) - chosen
    kept = (chosen > 0) & (slot < capacity)
    hit = kept[None, :] & (slot[None, :] == slot_iota)
    onehot = hit.astype(jnp.bfloat16)
    row_iota = jnp.arange(rows, dtype=jnp.int32)
    row_of_slot = jnp.sum(jnp.where(hit, row_iota[None, :], 0), axis=1)
    row_of_slot = jnp.where(jnp.any(hit, axis=1), row_of_slot, rows)
    packed = jnp.dot(onehot, normed, preferred_element_type=jnp.float32).astype(jnp.bfloat16)
    other = swapped(packed, "expert")
    both = jnp.where(me == 0, jnp.concatenate([packed, other], axis=0),
                     jnp.concatenate([other, packed], axis=0))
    partials = expert_part(both, gate_dev, up_dev, down_dev)
    mine = jnp.where(me == 0, partials[:capacity], partials[capacity:])
    theirs = jnp.where(me == 0, partials[capacity:], partials[:capacity])
    summed = mine.astype(jnp.float32) + swapped(theirs, "expert").astype(jnp.float32)
    share = jnp.dot(onehot.astype(jnp.float32), weight, precision=lax.Precision.HIGHEST)
    scaled = summed * share[:, None]
    h_rows = jnp.dot(onehot, current, preferred_element_type=jnp.float32)
    new_rows = (h_rows + scaled).astype(jnp.bfloat16)
    new_rows = passed_along(new_rows, "section", 1)
    where_rows = passed_along(row_of_slot, "section", 1)
    moved = jnp.concatenate([moved_near, moved_far], axis=0)
    out = moved.at[where_rows].set(new_rows, mode="drop", unique_indices=True)
    return out[None]


def solution(mesh):
    return jax.shard_map(
        local,
        mesh=mesh,
        in_specs=(
            P("section", "expert", None),
            P("section", None),
            P("section", None, None),
            P("section", None, "expert"),
            P("section", None, "expert"),
            P("section", "expert", None),
            P(None, "section", "expert", None),
        ),
        out_specs=P("section", "expert", None),
        check_vma=False,
    )
```

```python
import jax
import jax.numpy as jnp
from jax import lax
from jax.sharding import PartitionSpec as P


def passed_along(x, axis, by):
    devices = lax.axis_size(axis)
    return lax.ppermute(x, axis, [(i, (i + by) % devices) for i in range(devices)])


def swapped(x, axis):
    return lax.ppermute(x, axis, [(0, 1), (1, 0)])


def expert_part(piece, gate_dev, up_dev, down_dev):
    gate = jnp.dot(piece, gate_dev, preferred_element_type=jnp.float32)
    upper = jnp.dot(piece, up_dev, preferred_element_type=jnp.float32)
    active = (jax.nn.silu(gate) * upper).astype(jnp.bfloat16)
    partial_out = jnp.dot(active, down_dev, preferred_element_type=jnp.float32)
    return lax.optimization_barrier(partial_out.astype(jnp.bfloat16))


def local(state, norm_gain, router, w_gate, w_up, w_down, route_ids):
    gate_dev = w_gate[0]
    up_dev = w_up[0]
    down_dev = w_down[0]
    gain = norm_gain[0]
    table = router[0]
    current = state[0]
    moved = passed_along(current, "section", 1)
    rows = current.shape[0]
    capacity = rows // 8
    me = lax.axis_index("expert")
    slot_iota = jnp.arange(capacity)[:, None]
    expert_iota = jnp.arange(table.shape[1])
    h32 = current.astype(jnp.float32)
    var = jnp.mean(h32 * h32, axis=-1, keepdims=True)
    normed = (h32 * lax.rsqrt(var + 1e-06) * gain).astype(jnp.bfloat16)
    scores = jax.nn.sigmoid(jnp.dot(normed, table, preferred_element_type=jnp.float32))
    ids = route_ids[0, 0]
    picked = jnp.sum((ids[:, :, None] == expert_iota[None, None, :]).astype(jnp.float32), axis=1)
    weight = 2.5 * scores[:, 0] * picked[:, 0] / jnp.sum(scores * picked, axis=-1)
    chosen = jnp.sum((ids == 0).astype(jnp.int32), axis=-1)
    slot = jnp.cumsum(chosen) - chosen
    kept = (chosen > 0) & (slot < capacity)
    hit = kept[None, :] & (slot[None, :] == slot_iota)
    onehot = hit.astype(jnp.bfloat16)
    row_iota = jnp.arange(rows, dtype=jnp.int32)
    row_of_slot = jnp.sum(jnp.where(hit, row_iota[None, :], 0), axis=1)
    row_of_slot = jnp.where(jnp.any(hit, axis=1), row_of_slot, rows)
    packed = jnp.dot(onehot, normed, preferred_element_type=jnp.float32).astype(jnp.bfloat16)
    other = swapped(packed, "expert")
    both = jnp.where(me == 0, jnp.concatenate([packed, other], axis=0),
                     jnp.concatenate([other, packed], axis=0))
    partials = expert_part(both, gate_dev, up_dev, down_dev)
    mine = jnp.where(me == 0, partials[:capacity], partials[capacity:])
    theirs = jnp.where(me == 0, partials[capacity:], partials[:capacity])
    summed = mine.astype(jnp.float32) + swapped(theirs, "expert").astype(jnp.float32)
    share = jnp.dot(onehot.astype(jnp.float32), weight, precision=lax.Precision.HIGHEST)
    scaled = summed * share[:, None]
    h_rows = jnp.dot(onehot, current, preferred_element_type=jnp.float32)
    new_rows = (h_rows + scaled).astype(jnp.bfloat16)
    new_rows = passed_along(new_rows, "section", 1)
    where_rows = passed_along(row_of_slot, "section", 1)
    lands = where_rows[None, :] == row_iota[:, None]
    placed = jnp.dot(lands.astype(jnp.bfloat16), new_rows, preferred_element_type=jnp.float32)
    out = jnp.where(jnp.any(lands, axis=1)[:, None], placed.astype(jnp.bfloat16), moved)
    return out[None]


def solution(mesh):
    return jax.shard_map(
        local,
        mesh=mesh,
        in_specs=(
            P("section", "expert", None),
            P("section", None),
            P("section", None, None),
            P("section", None, "expert"),
            P("section", None, "expert"),
            P("section", "expert", None),
            P(None, "section", "expert", None),
        ),
        out_specs=P("section", "expert", None),
        check_vma=False,
    )
```

```python
import jax
import jax.numpy as jnp
from jax import lax
from jax.sharding import PartitionSpec as P


def passed_along(x, axis, by):
    devices = lax.axis_size(axis)
    return lax.ppermute(x, axis, [(i, (i + by) % devices) for i in range(devices)])


def swapped(x, axis):
    return lax.ppermute(x, axis, [(0, 1), (1, 0)])


def expert_part(piece, gate_dev, up_dev, down_dev):
    gate = jnp.dot(piece, gate_dev, preferred_element_type=jnp.float32)
    upper = jnp.dot(piece, up_dev, preferred_element_type=jnp.float32)
    active = (jax.nn.silu(gate) * upper).astype(jnp.bfloat16)
    partial_out = jnp.dot(active, down_dev, preferred_element_type=jnp.float32)
    return lax.optimization_barrier(partial_out.astype(jnp.bfloat16))


def local(state, norm_gain, router, w_gate, w_up, w_down, route_ids):
    gate_dev = w_gate[0]
    up_dev = w_up[0]
    down_dev = w_down[0]
    gain = norm_gain[0]
    table = router[0]
    current = state[0]
    rows = current.shape[0]
    capacity = rows // 8
    chosen = jnp.sum((route_ids[0, 0] == 0).astype(jnp.int32), axis=-1)
    slot = jnp.cumsum(chosen) - chosen
    kept = (chosen > 0) & (slot < capacity)
    stays = jnp.logical_not(kept).astype(jnp.int32)
    n_stay = jnp.sum(stays)
    place = jnp.where(kept, n_stay + slot, jnp.cumsum(stays) - stays)
    row_iota = jnp.arange(rows, dtype=jnp.int32)
    row_at = jnp.sum(jnp.where(place[None, :] == row_iota[:, None], row_iota[None, :], 0), axis=1)
    bulk = rows - capacity
    moved_bulk = passed_along(jnp.take(current, row_at[:bulk], axis=0, mode="clip"), "section", 1)
    me = lax.axis_index("expert")
    slot_iota = jnp.arange(capacity)[:, None]
    expert_iota = jnp.arange(table.shape[1])
    h32 = current.astype(jnp.float32)
    var = jnp.mean(h32 * h32, axis=-1, keepdims=True)
    normed = (h32 * lax.rsqrt(var + 1e-06) * gain).astype(jnp.bfloat16)
    scores = jax.nn.sigmoid(jnp.dot(normed, table, preferred_element_type=jnp.float32))
    ids = route_ids[0, 0]
    picked = jnp.sum((ids[:, :, None] == expert_iota[None, None, :]).astype(jnp.float32), axis=1)
    weight = 2.5 * scores[:, 0] * picked[:, 0] / jnp.sum(scores * picked, axis=-1)
    hit = kept[None, :] & (slot[None, :] == slot_iota)
    onehot = hit.astype(jnp.bfloat16)
    packed = jnp.dot(onehot, normed, preferred_element_type=jnp.float32).astype(jnp.bfloat16)
    other = swapped(packed, "expert")
    both = jnp.where(me == 0, jnp.concatenate([packed, other], axis=0),
                     jnp.concatenate([other, packed], axis=0))
    partials = expert_part(both, gate_dev, up_dev, down_dev)
    mine = jnp.where(me == 0, partials[:capacity], partials[capacity:])
    theirs = jnp.where(me == 0, partials[capacity:], partials[:capacity])
    summed = mine.astype(jnp.float32) + swapped(theirs, "expert").astype(jnp.float32)
    share = jnp.dot(onehot.astype(jnp.float32), weight, precision=lax.Precision.HIGHEST)
    scaled = summed * share[:, None]
    h_rows = jnp.dot(onehot, current, preferred_element_type=jnp.float32)
    new_rows = (h_rows + scaled).astype(jnp.bfloat16)
    spare = rows - n_stay
    tail_iota = jnp.arange(capacity, dtype=jnp.int32)
    left_over = jnp.take(current, row_at[bulk:], axis=0, mode="clip")
    shifted = jnp.take(new_rows, (tail_iota - (capacity - spare)) % capacity, axis=0, mode="clip")
    tail = jnp.where((tail_iota < capacity - spare)[:, None], left_over, shifted)
    tail = passed_along(tail, "section", 1)
    place = passed_along(place, "section", 1)
    out = jnp.take(jnp.concatenate([moved_bulk, tail], axis=0), place, axis=0, mode="clip")
    return out[None]


def solution(mesh):
    return jax.shard_map(
        local,
        mesh=mesh,
        in_specs=(
            P("section", "expert", None),
            P("section", None),
            P("section", None, None),
            P("section", None, "expert"),
            P("section", None, "expert"),
            P("section", "expert", None),
            P(None, "section", "expert", None),
        ),
        out_specs=P("section", "expert", None),
        check_vma=False,
    )
```

```python
import jax
import jax.numpy as jnp
from jax import lax
from jax.sharding import PartitionSpec as P


def passed_along(x, axis, by):
    devices = lax.axis_size(axis)
    return lax.ppermute(x, axis, [(i, (i + by) % devices) for i in range(devices)])


def swapped(x, axis):
    return lax.ppermute(x, axis, [(0, 1), (1, 0)])


def expert_part(piece, gate_dev, up_dev, down_dev):
    gate = jnp.dot(piece, gate_dev, preferred_element_type=jnp.float32)
    upper = jnp.dot(piece, up_dev, preferred_element_type=jnp.float32)
    active = (jax.nn.silu(gate) * upper).astype(jnp.bfloat16)
    partial_out = jnp.dot(active, down_dev, preferred_element_type=jnp.float32)
    return lax.optimization_barrier(partial_out.astype(jnp.bfloat16))


def local(state, norm_gain, router, w_gate, w_up, w_down, route_ids):
    gate_dev = w_gate[0]
    up_dev = w_up[0]
    down_dev = w_down[0]
    gain = norm_gain[0]
    table = router[0]
    current = state[0]
    rows = current.shape[0]
    capacity = rows // 8
    bulk = rows - capacity
    chosen = jnp.sum((route_ids[0, 0] == 0).astype(jnp.int32), axis=-1)
    slot = jnp.cumsum(chosen) - chosen
    kept = (chosen > 0) & (slot < capacity)
    row_iota = jnp.arange(rows, dtype=jnp.int32)
    hole = kept & (row_iota < bulk)
    free = jnp.logical_not(kept) & (row_iota >= bulk)
    hole_rank = jnp.cumsum(hole.astype(jnp.int32)) - hole.astype(jnp.int32)
    free_rank = jnp.cumsum(free.astype(jnp.int32)) - free.astype(jnp.int32)
    n_holes = jnp.sum(hole.astype(jnp.int32))
    used = free & (free_rank < n_holes)
    top_hole, tail_used = hole[:bulk], used[bulk:]
    pairs = top_hole[:, None] & tail_used[None, :] & (hole_rank[:bulk, None] == free_rank[None, bulk:])
    tail_iota = jnp.arange(capacity, dtype=jnp.int32)
    top_mate = jnp.where(top_hole, jnp.sum(jnp.where(pairs, tail_iota[None, :], 0), axis=1), -1)
    tail_mate = jnp.where(tail_used, jnp.sum(jnp.where(pairs, row_iota[:bulk, None], 0), axis=0), -1)
    fill = jnp.dot(pairs.astype(jnp.bfloat16), current[bulk:], preferred_element_type=jnp.float32)
    with jax.named_scope("bulk"):
        first = jnp.where(top_hole[:, None], fill.astype(jnp.bfloat16), current[:bulk])
        moved_first = passed_along(first, "section", 1)
    me = lax.axis_index("expert")
    slot_iota = jnp.arange(capacity)[:, None]
    expert_iota = jnp.arange(table.shape[1])
    h32 = current.astype(jnp.float32)
    var = jnp.mean(h32 * h32, axis=-1, keepdims=True)
    normed = (h32 * lax.rsqrt(var + 1e-06) * gain).astype(jnp.bfloat16)
    scores = jax.nn.sigmoid(jnp.dot(normed, table, preferred_element_type=jnp.float32))
    ids = route_ids[0, 0]
    picked = jnp.sum((ids[:, :, None] == expert_iota[None, None, :]).astype(jnp.float32), axis=1)
    weight = 2.5 * scores[:, 0] * picked[:, 0] / jnp.sum(scores * picked, axis=-1)
    hit = kept[None, :] & (slot[None, :] == slot_iota)
    onehot = hit.astype(jnp.bfloat16)
    packed = jnp.dot(onehot, normed, preferred_element_type=jnp.float32).astype(jnp.bfloat16)
    other = swapped(packed, "expert")
    both = jnp.where(me == 0, jnp.concatenate([packed, other], axis=0),
                     jnp.concatenate([other, packed], axis=0))
    partials = expert_part(both, gate_dev, up_dev, down_dev)
    mine = jnp.where(me == 0, partials[:capacity], partials[capacity:])
    theirs = jnp.where(me == 0, partials[capacity:], partials[:capacity])
    summed = mine.astype(jnp.float32) + swapped(theirs, "expert").astype(jnp.float32)
    share = jnp.dot(onehot.astype(jnp.float32), weight, precision=lax.Precision.HIGHEST)
    scaled = summed * share[:, None]
    h_rows = jnp.dot(onehot, current, preferred_element_type=jnp.float32)
    new_rows = (h_rows + scaled).astype(jnp.bfloat16)
    hole_slot = jnp.sum(jnp.where(pairs, slot[:bulk, None], 0), axis=0)
    tail_slot = jnp.where(kept[bulk:], slot[bulk:], jnp.where(tail_used, hole_slot, -1))
    carry = (tail_slot[:, None] == tail_iota[None, :]).astype(jnp.bfloat16)
    carried = jnp.dot(carry, new_rows, preferred_element_type=jnp.float32).astype(jnp.bfloat16)
    second = jnp.where((tail_slot >= 0)[:, None], carried, current[bulk:])
    second = passed_along(second, "section", 1)
    mate = passed_along(jnp.concatenate([top_mate, tail_mate]), "section", 1)
    top_mate, tail_mate = mate[:bulk], mate[bulk:]
    back_top = (top_mate[:, None] == tail_iota[None, :]).astype(jnp.bfloat16)
    top = jnp.where((top_mate >= 0)[:, None],
                    jnp.dot(back_top, second, preferred_element_type=jnp.float32).astype(jnp.bfloat16),
                    moved_first)
    back_tail = (tail_mate[:, None] == row_iota[None, :bulk]).astype(jnp.bfloat16)
    low = jnp.where((tail_mate >= 0)[:, None],
                    jnp.dot(back_tail, moved_first, preferred_element_type=jnp.float32).astype(jnp.bfloat16),
                    second)
    out = jnp.concatenate([top, low], axis=0)
    return out[None]


def solution(mesh):
    return jax.shard_map(
        local,
        mesh=mesh,
        in_specs=(
            P("section", "expert", None),
            P("section", None),
            P("section", None, None),
            P("section", None, "expert"),
            P("section", None, "expert"),
            P("section", "expert", None),
            P(None, "section", "expert", None),
        ),
        out_specs=P("section", "expert", None),
        check_vma=False,
    )
```

```python
import jax
import jax.numpy as jnp
from jax import lax
from jax.sharding import PartitionSpec as P


def passed_along(x, axis, by):
    devices = lax.axis_size(axis)
    return lax.ppermute(x, axis, [(i, (i + by) % devices) for i in range(devices)])


def swapped(x, axis):
    return lax.ppermute(x, axis, [(0, 1), (1, 0)])


def expert_part(piece, gate_dev, up_dev, down_dev):
    gate = jnp.dot(piece, gate_dev, preferred_element_type=jnp.float32)
    upper = jnp.dot(piece, up_dev, preferred_element_type=jnp.float32)
    active = (jax.nn.silu(gate) * upper).astype(jnp.bfloat16)
    partial_out = jnp.dot(active, down_dev, preferred_element_type=jnp.float32)
    return lax.optimization_barrier(partial_out.astype(jnp.bfloat16))


def local(state, norm_gain, router, w_gate, w_up, w_down, route_ids):
    gate_dev = w_gate[0]
    up_dev = w_up[0]
    down_dev = w_down[0]
    gain = norm_gain[0]
    table = router[0]
    current = state[0]
    rows = current.shape[0]
    capacity = rows // 8
    bulk = rows - capacity
    chosen = jnp.sum((route_ids[0, 0] == 0).astype(jnp.int32), axis=-1)
    slot = jnp.cumsum(chosen) - chosen
    kept = (chosen > 0) & (slot < capacity)
    row_iota = jnp.arange(rows, dtype=jnp.int32)
    hole = kept & (row_iota < bulk)
    free = jnp.logical_not(kept) & (row_iota >= bulk)
    hole_rank = jnp.cumsum(hole.astype(jnp.int32)) - hole.astype(jnp.int32)
    free_rank = jnp.cumsum(free.astype(jnp.int32)) - free.astype(jnp.int32)
    n_holes = jnp.sum(hole.astype(jnp.int32))
    used = free & (free_rank < n_holes)
    top_hole, tail_used = hole[:bulk], used[bulk:]
    pairs = top_hole[:, None] & tail_used[None, :] & (hole_rank[:bulk, None] == free_rank[None, bulk:])
    tail_iota = jnp.arange(capacity, dtype=jnp.int32)
    top_mate = jnp.where(top_hole, jnp.sum(jnp.where(pairs, tail_iota[None, :], 0), axis=1), -1)
    tail_mate = jnp.where(tail_used, jnp.sum(jnp.where(pairs, row_iota[:bulk, None], 0), axis=0), -1)
    fill = jnp.dot(pairs.astype(jnp.bfloat16), current[bulk:], preferred_element_type=jnp.float32)
    with jax.named_scope("bulk"):
        first = jnp.where(top_hole[:, None], fill.astype(jnp.bfloat16), current[:bulk])
        moved_first = passed_along(first, "section", 1)
    me = lax.axis_index("expert")
    slot_iota = jnp.arange(capacity)[:, None]
    expert_iota = jnp.arange(table.shape[1])
    h32 = current.astype(jnp.float32)
    var = jnp.mean(h32 * h32, axis=-1, keepdims=True)
    normed = (h32 * lax.rsqrt(var + 1e-06) * gain).astype(jnp.bfloat16)
    scores = jax.nn.sigmoid(jnp.dot(normed, table, preferred_element_type=jnp.float32))
    ids = route_ids[0, 0]
    picked = jnp.sum((ids[:, :, None] == expert_iota[None, None, :]).astype(jnp.float32), axis=1)
    weight = 2.5 * scores[:, 0] * picked[:, 0] / jnp.sum(scores * picked, axis=-1)
    hit = kept[None, :] & (slot[None, :] == slot_iota)
    onehot = hit.astype(jnp.bfloat16)
    packed = jnp.dot(onehot, normed, preferred_element_type=jnp.float32).astype(jnp.bfloat16)
    other = swapped(packed, "expert")
    both = jnp.where(me == 0, jnp.concatenate([packed, other], axis=0),
                     jnp.concatenate([other, packed], axis=0))
    partials = expert_part(both, gate_dev, up_dev, down_dev)
    mine = jnp.where(me == 0, partials[:capacity], partials[capacity:])
    theirs = jnp.where(me == 0, partials[capacity:], partials[:capacity])
    summed = mine.astype(jnp.float32) + swapped(theirs, "expert").astype(jnp.float32)
    share = jnp.dot(onehot.astype(jnp.float32), weight, precision=lax.Precision.HIGHEST)
    scaled = summed * share[:, None]
    h_rows = jnp.dot(onehot, current, preferred_element_type=jnp.float32)
    new_rows = (h_rows + scaled).astype(jnp.bfloat16)
    hole_slot = jnp.sum(jnp.where(pairs, slot[:bulk, None], 0), axis=0)
    tail_slot = jnp.where(kept[bulk:], slot[bulk:], jnp.where(tail_used, hole_slot, -1))
    carry = (tail_slot[:, None] == tail_iota[None, :]).astype(jnp.bfloat16)
    carried = jnp.dot(carry, new_rows, preferred_element_type=jnp.float32).astype(jnp.bfloat16)
    second = jnp.where((tail_slot >= 0)[:, None], carried, current[bulk:])
    second = passed_along(second, "section", 1)
    mate = passed_along(jnp.concatenate([top_mate, tail_mate]), "section", 1)
    tail_mate = mate[bulk:]
    top_mate = jnp.where(row_iota < bulk, mate, -1)
    back_top = (top_mate[:, None] == tail_iota[None, :]).astype(jnp.bfloat16)
    out = jnp.where((top_mate >= 0)[:, None],
                    jnp.dot(back_top, second, preferred_element_type=jnp.float32).astype(jnp.bfloat16),
                    jnp.concatenate([moved_first, second], axis=0))
    back_tail = (tail_mate[:, None] == row_iota[None, :bulk]).astype(jnp.bfloat16)
    low = jnp.where((tail_mate >= 0)[:, None],
                    jnp.dot(back_tail, moved_first, preferred_element_type=jnp.float32).astype(jnp.bfloat16),
                    second)
    out = lax.dynamic_update_slice(out, low, (bulk, 0))
    return out[None]


def solution(mesh):
    return jax.shard_map(
        local,
        mesh=mesh,
        in_specs=(
            P("section", "expert", None),
            P("section", None),
            P("section", None, None),
            P("section", None, "expert"),
            P("section", None, "expert"),
            P("section", "expert", None),
            P(None, "section", "expert", None),
        ),
        out_specs=P("section", "expert", None),
        check_vma=False,
    )
```

```python
import jax
import jax.numpy as jnp
from jax import lax
from jax.sharding import PartitionSpec as P

LEAD_ROWS = 256


def passed_along(x, axis, by):
    devices = lax.axis_size(axis)
    return lax.ppermute(x, axis, [(i, (i + by) % devices) for i in range(devices)])


def swapped(x, axis):
    return lax.ppermute(x, axis, [(0, 1), (1, 0)])


def expert_part(piece, gate_dev, up_dev, down_dev):
    gate = jnp.dot(piece, gate_dev, preferred_element_type=jnp.float32)
    upper = jnp.dot(piece, up_dev, preferred_element_type=jnp.float32)
    active = (jax.nn.silu(gate) * upper).astype(jnp.bfloat16)
    partial_out = jnp.dot(active, down_dev, preferred_element_type=jnp.float32)
    return lax.optimization_barrier(partial_out.astype(jnp.bfloat16))


def local(state, norm_gain, router, w_gate, w_up, w_down, route_ids):
    gate_dev = w_gate[0]
    up_dev = w_up[0]
    down_dev = w_down[0]
    gain = norm_gain[0]
    table = router[0]
    current = state[0]
    rows = current.shape[0]
    capacity = rows // 8
    bulk = rows - capacity
    chosen = jnp.sum((route_ids[0, 0] == 0).astype(jnp.int32), axis=-1)
    slot = jnp.cumsum(chosen) - chosen
    kept = (chosen > 0) & (slot < capacity)
    row_iota = jnp.arange(rows, dtype=jnp.int32)
    hole = kept & (row_iota < bulk)
    free = jnp.logical_not(kept) & (row_iota >= bulk)
    hole_rank = jnp.cumsum(hole.astype(jnp.int32)) - hole.astype(jnp.int32)
    free_rank = jnp.cumsum(free.astype(jnp.int32)) - free.astype(jnp.int32)
    n_holes = jnp.sum(hole.astype(jnp.int32))
    used = free & (free_rank < n_holes)
    top_hole, tail_used = hole[:bulk], used[bulk:]
    pairs = top_hole[:, None] & tail_used[None, :] & (hole_rank[:bulk, None] == free_rank[None, bulk:])
    tail_iota = jnp.arange(capacity, dtype=jnp.int32)
    top_mate = jnp.where(top_hole, jnp.sum(jnp.where(pairs, tail_iota[None, :], 0), axis=1), -1)
    tail_mate = jnp.where(tail_used, jnp.sum(jnp.where(pairs, row_iota[:bulk, None], 0), axis=0), -1)
    cuts = [(0, LEAD_ROWS), (LEAD_ROWS, bulk)]
    moved_first = []
    for a, b in cuts:
        fill = jnp.dot(pairs[a:b].astype(jnp.bfloat16), current[bulk:], preferred_element_type=jnp.float32)
        first = jnp.where(top_hole[a:b, None], fill.astype(jnp.bfloat16), current[a:b])
        moved_first.append(passed_along(first, "section", 1))
    me = lax.axis_index("expert")
    slot_iota = jnp.arange(capacity)[:, None]
    expert_iota = jnp.arange(table.shape[1])
    h32 = current.astype(jnp.float32)
    var = jnp.mean(h32 * h32, axis=-1, keepdims=True)
    normed = (h32 * lax.rsqrt(var + 1e-06) * gain).astype(jnp.bfloat16)
    scores = jax.nn.sigmoid(jnp.dot(normed, table, preferred_element_type=jnp.float32))
    ids = route_ids[0, 0]
    picked = jnp.sum((ids[:, :, None] == expert_iota[None, None, :]).astype(jnp.float32), axis=1)
    weight = 2.5 * scores[:, 0] * picked[:, 0] / jnp.sum(scores * picked, axis=-1)
    hit = kept[None, :] & (slot[None, :] == slot_iota)
    onehot = hit.astype(jnp.bfloat16)
    packed = jnp.dot(onehot, normed, preferred_element_type=jnp.float32).astype(jnp.bfloat16)
    other = swapped(packed, "expert")
    both = jnp.where(me == 0, jnp.concatenate([packed, other], axis=0),
                     jnp.concatenate([other, packed], axis=0))
    partials = expert_part(both, gate_dev, up_dev, down_dev)
    mine = jnp.where(me == 0, partials[:capacity], partials[capacity:])
    theirs = jnp.where(me == 0, partials[capacity:], partials[:capacity])
    summed = mine.astype(jnp.float32) + swapped(theirs, "expert").astype(jnp.float32)
    share = jnp.dot(onehot.astype(jnp.float32), weight, precision=lax.Precision.HIGHEST)
    scaled = summed * share[:, None]
    h_rows = jnp.dot(onehot, current, preferred_element_type=jnp.float32)
    new_rows = (h_rows + scaled).astype(jnp.bfloat16)
    hole_slot = jnp.sum(jnp.where(pairs, slot[:bulk, None], 0), axis=0)
    tail_slot = jnp.where(kept[bulk:], slot[bulk:], jnp.where(tail_used, hole_slot, -1))
    carry = (tail_slot[:, None] == tail_iota[None, :]).astype(jnp.bfloat16)
    carried = jnp.dot(carry, new_rows, preferred_element_type=jnp.float32).astype(jnp.bfloat16)
    second = jnp.where((tail_slot >= 0)[:, None], carried, current[bulk:])
    second = passed_along(second, "section", 1)
    mate = passed_along(jnp.concatenate([top_mate, tail_mate]), "section", 1)
    tail_mate = mate[bulk:]
    top_mate = jnp.where(row_iota < bulk, mate, -1)
    back_top = (top_mate[:, None] == tail_iota[None, :]).astype(jnp.bfloat16)
    out = jnp.where((top_mate >= 0)[:, None],
                    jnp.dot(back_top, second, preferred_element_type=jnp.float32).astype(jnp.bfloat16),
                    jnp.concatenate(moved_first + [second], axis=0))
    back_tail = (tail_mate[:, None] == row_iota[None, :bulk]).astype(jnp.bfloat16)
    low = jnp.where((tail_mate >= 0)[:, None],
                    sum(jnp.dot(back_tail[:, a:b], part, preferred_element_type=jnp.float32)
                        for (a, b), part in zip(cuts, moved_first)).astype(jnp.bfloat16),
                    second)
    out = lax.dynamic_update_slice(out, low, (bulk, 0))
    return out[None]


def solution(mesh):
    return jax.shard_map(
        local,
        mesh=mesh,
        in_specs=(
            P("section", "expert", None),
            P("section", None),
            P("section", None, None),
            P("section", None, "expert"),
            P("section", None, "expert"),
            P("section", "expert", None),
            P(None, "section", "expert", None),
        ),
        out_specs=P("section", "expert", None),
        check_vma=False,
    )
```

```python
import jax
import jax.numpy as jnp
from jax import lax
from jax.sharding import PartitionSpec as P

LEAD_ROWS = 64


def passed_along(x, axis, by):
    devices = lax.axis_size(axis)
    return lax.ppermute(x, axis, [(i, (i + by) % devices) for i in range(devices)])


def swapped(x, axis):
    return lax.ppermute(x, axis, [(0, 1), (1, 0)])


def expert_part(piece, gate_dev, up_dev, down_dev):
    gate = jnp.dot(piece, gate_dev, preferred_element_type=jnp.float32)
    upper = jnp.dot(piece, up_dev, preferred_element_type=jnp.float32)
    active = (jax.nn.silu(gate) * upper).astype(jnp.bfloat16)
    partial_out = jnp.dot(active, down_dev, preferred_element_type=jnp.float32)
    return lax.optimization_barrier(partial_out.astype(jnp.bfloat16))


def local(state, norm_gain, router, w_gate, w_up, w_down, route_ids):
    gate_dev = w_gate[0]
    up_dev = w_up[0]
    down_dev = w_down[0]
    gain = norm_gain[0]
    table = router[0]
    current = state[0]
    rows = current.shape[0]
    capacity = rows // 8
    bulk = rows - capacity
    chosen = jnp.sum((route_ids[0, 0] == 0).astype(jnp.int32), axis=-1)
    slot = jnp.cumsum(chosen) - chosen
    kept = (chosen > 0) & (slot < capacity)
    row_iota = jnp.arange(rows, dtype=jnp.int32)
    hole = kept & (row_iota < bulk)
    free = jnp.logical_not(kept) & (row_iota >= bulk)
    hole_rank = jnp.cumsum(hole.astype(jnp.int32)) - hole.astype(jnp.int32)
    free_rank = jnp.cumsum(free.astype(jnp.int32)) - free.astype(jnp.int32)
    n_holes = jnp.sum(hole.astype(jnp.int32))
    used = free & (free_rank < n_holes)
    top_hole, tail_used = hole[:bulk], used[bulk:]
    pairs = top_hole[:, None] & tail_used[None, :] & (hole_rank[:bulk, None] == free_rank[None, bulk:])
    tail_iota = jnp.arange(capacity, dtype=jnp.int32)
    top_mate = jnp.where(top_hole, jnp.sum(jnp.where(pairs, tail_iota[None, :], 0), axis=1), -1)
    tail_mate = jnp.where(tail_used, jnp.sum(jnp.where(pairs, row_iota[:bulk, None], 0), axis=0), -1)
    cuts = [(0, LEAD_ROWS), (LEAD_ROWS, bulk)]
    moved_first = []
    for a, b in cuts:
        fill = jnp.dot(pairs[a:b].astype(jnp.bfloat16), current[bulk:], preferred_element_type=jnp.float32)
        first = jnp.where(top_hole[a:b, None], fill.astype(jnp.bfloat16), current[a:b])
        moved_first.append(passed_along(first, "section", 1))
    me = lax.axis_index("expert")
    slot_iota = jnp.arange(capacity)[:, None]
    expert_iota = jnp.arange(table.shape[1])
    h32 = current.astype(jnp.float32)
    var = jnp.mean(h32 * h32, axis=-1, keepdims=True)
    normed = (h32 * lax.rsqrt(var + 1e-06) * gain).astype(jnp.bfloat16)
    scores = jax.nn.sigmoid(jnp.dot(normed, table, preferred_element_type=jnp.float32))
    ids = route_ids[0, 0]
    picked = jnp.sum((ids[:, :, None] == expert_iota[None, None, :]).astype(jnp.float32), axis=1)
    weight = 2.5 * scores[:, 0] * picked[:, 0] / jnp.sum(scores * picked, axis=-1)
    hit = kept[None, :] & (slot[None, :] == slot_iota)
    onehot = hit.astype(jnp.bfloat16)
    packed = jnp.dot(onehot, normed, preferred_element_type=jnp.float32).astype(jnp.bfloat16)
    other = swapped(packed, "expert")
    both = jnp.where(me == 0, jnp.concatenate([packed, other], axis=0),
                     jnp.concatenate([other, packed], axis=0))
    partials = expert_part(both, gate_dev, up_dev, down_dev)
    mine = jnp.where(me == 0, partials[:capacity], partials[capacity:])
    theirs = jnp.where(me == 0, partials[capacity:], partials[:capacity])
    summed = mine.astype(jnp.float32) + swapped(theirs, "expert").astype(jnp.float32)
    share = jnp.dot(onehot.astype(jnp.float32), weight, precision=lax.Precision.HIGHEST)
    scaled = summed * share[:, None]
    h_rows = jnp.dot(onehot, current, preferred_element_type=jnp.float32)
    new_rows = (h_rows + scaled).astype(jnp.bfloat16)
    hole_slot = jnp.sum(jnp.where(pairs, slot[:bulk, None], 0), axis=0)
    tail_slot = jnp.where(kept[bulk:], slot[bulk:], jnp.where(tail_used, hole_slot, -1))
    carry = (tail_slot[:, None] == tail_iota[None, :]).astype(jnp.bfloat16)
    carried = jnp.dot(carry, new_rows, preferred_element_type=jnp.float32).astype(jnp.bfloat16)
    second = jnp.where((tail_slot >= 0)[:, None], carried, current[bulk:])
    second, mate = lax.optimization_barrier((second, jnp.concatenate([top_mate, tail_mate])))
    second = passed_along(second, "section", 1)
    mate = passed_along(mate, "section", 1)
    tail_mate = mate[bulk:]
    top_mate = jnp.where(row_iota < bulk, mate, -1)
    back_top = (top_mate[:, None] == tail_iota[None, :]).astype(jnp.bfloat16)
    out = jnp.where((top_mate >= 0)[:, None],
                    jnp.dot(back_top, second, preferred_element_type=jnp.float32).astype(jnp.bfloat16),
                    jnp.concatenate(moved_first + [second], axis=0))
    back_tail = (tail_mate[:, None] == row_iota[None, :bulk]).astype(jnp.bfloat16)
    low = jnp.where((tail_mate >= 0)[:, None],
                    sum(jnp.dot(back_tail[:, a:b], part, preferred_element_type=jnp.float32)
                        for (a, b), part in zip(cuts, moved_first)).astype(jnp.bfloat16),
                    second)
    out = lax.dynamic_update_slice(out, low, (bulk, 0))
    return out[None]


def solution(mesh):
    return jax.shard_map(
        local,
        mesh=mesh,
        in_specs=(
            P("section", "expert", None),
            P("section", None),
            P("section", None, None),
            P("section", None, "expert"),
            P("section", None, "expert"),
            P("section", "expert", None),
            P(None, "section", "expert", None),
        ),
        out_specs=P("section", "expert", None),
        check_vma=False,
    )
```

```python
import jax
import jax.numpy as jnp
from jax import lax
from jax.sharding import PartitionSpec as P

LEAD_ROWS = 64


def passed_along(x, axis, by):
    devices = lax.axis_size(axis)
    return lax.ppermute(x, axis, [(i, (i + by) % devices) for i in range(devices)])


def swapped(x, axis):
    return lax.ppermute(x, axis, [(0, 1), (1, 0)])


def expert_part(piece, gate_dev, up_dev, down_dev):
    gate = jnp.dot(piece, gate_dev, preferred_element_type=jnp.float32)
    upper = jnp.dot(piece, up_dev, preferred_element_type=jnp.float32)
    active = (jax.nn.silu(gate) * upper).astype(jnp.bfloat16)
    partial_out = jnp.dot(active, down_dev, preferred_element_type=jnp.float32)
    return lax.optimization_barrier(partial_out.astype(jnp.bfloat16))


def local(state, norm_gain, router, w_gate, w_up, w_down, route_ids):
    gate_dev = w_gate[0]
    up_dev = w_up[0]
    down_dev = w_down[0]
    gain = norm_gain[0]
    table = router[0]
    current = state[0]
    rows = current.shape[0]
    capacity = rows // 8
    bulk = rows - capacity
    chosen = jnp.sum((route_ids[0, 0] == 0).astype(jnp.int32), axis=-1)
    row_iota = jnp.arange(rows, dtype=jnp.int32)
    before = (row_iota[None, :] < row_iota[:, None]).astype(jnp.bfloat16)

    def earlier(*cols):
        stack = jnp.stack(cols, axis=1).astype(jnp.bfloat16)
        sums = jnp.dot(before, stack, preferred_element_type=jnp.float32).astype(jnp.int32)
        return [sums[:, k] for k in range(len(cols))]

    (slot,) = earlier(chosen)
    kept = (chosen > 0) & (slot < capacity)
    hole = kept & (row_iota < bulk)
    free = jnp.logical_not(kept) & (row_iota >= bulk)
    hole_rank, free_rank = earlier(hole, free)
    n_holes = jnp.sum(hole.astype(jnp.int32))
    used = free & (free_rank < n_holes)
    top_hole, tail_used = hole[:bulk], used[bulk:]
    pairs = top_hole[:, None] & tail_used[None, :] & (hole_rank[:bulk, None] == free_rank[None, bulk:])
    tail_iota = jnp.arange(capacity, dtype=jnp.int32)
    top_mate = jnp.where(top_hole, jnp.sum(jnp.where(pairs, tail_iota[None, :], 0), axis=1), -1)
    tail_mate = jnp.where(tail_used, jnp.sum(jnp.where(pairs, row_iota[:bulk, None], 0), axis=0), -1)
    cuts = [(0, LEAD_ROWS), (LEAD_ROWS, bulk)]
    moved_first = []
    for a, b in cuts:
        fill = jnp.dot(pairs[a:b].astype(jnp.bfloat16), current[bulk:], preferred_element_type=jnp.float32)
        first = jnp.where(top_hole[a:b, None], fill.astype(jnp.bfloat16), current[a:b])
        moved_first.append(passed_along(first, "section", 1))
    me = lax.axis_index("expert")
    slot_iota = jnp.arange(capacity)[:, None]
    expert_iota = jnp.arange(table.shape[1])
    h32 = current.astype(jnp.float32)
    var = jnp.mean(h32 * h32, axis=-1, keepdims=True)
    normed = (h32 * lax.rsqrt(var + 1e-06) * gain).astype(jnp.bfloat16)
    scores = jax.nn.sigmoid(jnp.dot(normed, table, preferred_element_type=jnp.float32))
    ids = route_ids[0, 0]
    picked = jnp.sum((ids[:, :, None] == expert_iota[None, None, :]).astype(jnp.float32), axis=1)
    weight = 2.5 * scores[:, 0] * picked[:, 0] / jnp.sum(scores * picked, axis=-1)
    hit = kept[None, :] & (slot[None, :] == slot_iota)
    onehot = hit.astype(jnp.bfloat16)
    packed = jnp.dot(onehot, normed, preferred_element_type=jnp.float32).astype(jnp.bfloat16)
    other = swapped(packed, "expert")
    both = jnp.where(me == 0, jnp.concatenate([packed, other], axis=0),
                     jnp.concatenate([other, packed], axis=0))
    partials = expert_part(both, gate_dev, up_dev, down_dev)
    mine = jnp.where(me == 0, partials[:capacity], partials[capacity:])
    theirs = jnp.where(me == 0, partials[capacity:], partials[:capacity])
    summed = mine.astype(jnp.float32) + swapped(theirs, "expert").astype(jnp.float32)
    share = jnp.dot(onehot.astype(jnp.float32), weight, precision=lax.Precision.HIGHEST)
    scaled = summed * share[:, None]
    h_rows = jnp.dot(onehot, current, preferred_element_type=jnp.float32)
    new_rows = (h_rows + scaled).astype(jnp.bfloat16)
    hole_slot = jnp.sum(jnp.where(pairs, slot[:bulk, None], 0), axis=0)
    tail_slot = jnp.where(kept[bulk:], slot[bulk:], jnp.where(tail_used, hole_slot, -1))
    carry = (tail_slot[:, None] == tail_iota[None, :]).astype(jnp.bfloat16)
    carried = jnp.dot(carry, new_rows, preferred_element_type=jnp.float32).astype(jnp.bfloat16)
    second = jnp.where((tail_slot >= 0)[:, None], carried, current[bulk:])
    second, mate = lax.optimization_barrier((second, jnp.concatenate([top_mate, tail_mate])))
    second = passed_along(second, "section", 1)
    mate = passed_along(mate, "section", 1)
    tail_mate = mate[bulk:]
    top_mate = jnp.where(row_iota < bulk, mate, -1)
    back_top = (top_mate[:, None] == tail_iota[None, :]).astype(jnp.bfloat16)
    out = jnp.where((top_mate >= 0)[:, None],
                    jnp.dot(back_top, second, preferred_element_type=jnp.float32).astype(jnp.bfloat16),
                    jnp.concatenate(moved_first + [second], axis=0))
    back_tail = (tail_mate[:, None] == row_iota[None, :bulk]).astype(jnp.bfloat16)
    low = jnp.where((tail_mate >= 0)[:, None],
                    sum(jnp.dot(back_tail[:, a:b], part, preferred_element_type=jnp.float32)
                        for (a, b), part in zip(cuts, moved_first)).astype(jnp.bfloat16),
                    second)
    out = lax.dynamic_update_slice(out, low, (bulk, 0))
    return out[None]


def solution(mesh):
    return jax.shard_map(
        local,
        mesh=mesh,
        in_specs=(
            P("section", "expert", None),
            P("section", None),
            P("section", None, None),
            P("section", None, "expert"),
            P("section", None, "expert"),
            P("section", "expert", None),
            P(None, "section", "expert", None),
        ),
        out_specs=P("section", "expert", None),
        check_vma=False,
    )
```

```python
import jax
import jax.numpy as jnp
from jax import lax
from jax.sharding import PartitionSpec as P

LEAD_ROWS = 64


def passed_along(x, axis, by):
    devices = lax.axis_size(axis)
    return lax.ppermute(x, axis, [(i, (i + by) % devices) for i in range(devices)])


def swapped(x, axis):
    return lax.ppermute(x, axis, [(0, 1), (1, 0)])


def expert_part(piece, gate_dev, up_dev, down_dev):
    gate = jnp.dot(piece, gate_dev, preferred_element_type=jnp.float32)
    upper = jnp.dot(piece, up_dev, preferred_element_type=jnp.float32)
    active = (jax.nn.silu(gate) * upper).astype(jnp.bfloat16)
    partial_out = jnp.dot(active, down_dev, preferred_element_type=jnp.float32)
    return lax.optimization_barrier(partial_out.astype(jnp.bfloat16))


def local(state, norm_gain, router, w_gate, w_up, w_down, route_ids):
    gate_dev = w_gate[0]
    up_dev = w_up[0]
    down_dev = w_down[0]
    gain = norm_gain[0]
    table = router[0]
    current = state[0]
    rows = current.shape[0]
    capacity = rows // 8
    bulk = rows - capacity
    chosen = jnp.sum((route_ids[0, 0] == 0).astype(jnp.int32), axis=-1)
    row_iota = jnp.arange(rows, dtype=jnp.int32)
    before = (row_iota[None, :] < row_iota[:, None]).astype(jnp.bfloat16)

    def earlier(*cols):
        stack = jnp.stack(cols, axis=1).astype(jnp.bfloat16)
        sums = jnp.dot(before, stack, preferred_element_type=jnp.float32).astype(jnp.int32)
        return [sums[:, k] for k in range(len(cols))]

    (slot,) = earlier(chosen)
    kept = (chosen > 0) & (slot < capacity)
    hole = kept & (row_iota < bulk)
    free = jnp.logical_not(kept) & (row_iota >= bulk)
    hole_rank, free_rank = earlier(hole, free)
    n_holes = jnp.sum(hole.astype(jnp.int32))
    used = free & (free_rank < n_holes)
    top_hole, tail_used = hole[:bulk], used[bulk:]
    pairs = top_hole[:, None] & tail_used[None, :] & (hole_rank[:bulk, None] == free_rank[None, bulk:])
    tail_iota = jnp.arange(capacity, dtype=jnp.int32)
    top_mate = jnp.where(top_hole, jnp.sum(jnp.where(pairs, tail_iota[None, :], 0), axis=1), -1)
    tail_mate = jnp.where(tail_used, jnp.sum(jnp.where(pairs, row_iota[:bulk, None], 0), axis=0), -1)
    cuts = [(0, LEAD_ROWS), (LEAD_ROWS, bulk)]
    moved_first = []
    for a, b in cuts:
        fill = jnp.dot(pairs[a:b].astype(jnp.bfloat16), current[bulk:], preferred_element_type=jnp.float32)
        first = jnp.where(top_hole[a:b, None], fill.astype(jnp.bfloat16), current[a:b])
        moved_first.append(passed_along(first, "section", 1))
    me = lax.axis_index("expert")
    slot_iota = jnp.arange(capacity)[:, None]
    expert_iota = jnp.arange(table.shape[1])
    h32 = current.astype(jnp.float32)
    var = jnp.mean(h32 * h32, axis=-1, keepdims=True)
    normed = (h32 * lax.rsqrt(var + 1e-06) * gain).astype(jnp.bfloat16)
    scores = jax.nn.sigmoid(jnp.dot(normed, table, preferred_element_type=jnp.float32))
    ids = route_ids[0, 0]
    picked = jnp.sum((ids[:, :, None] == expert_iota[None, None, :]).astype(jnp.float32), axis=1)
    weight = 2.5 * scores[:, 0] * picked[:, 0] / jnp.sum(scores * picked, axis=-1)
    hit = kept[None, :] & (slot[None, :] == slot_iota)
    onehot = hit.astype(jnp.bfloat16)
    packed = jnp.dot(onehot, normed, preferred_element_type=jnp.float32).astype(jnp.bfloat16)
    other = swapped(packed, "expert")
    both = jnp.where(me == 0, jnp.concatenate([packed, other], axis=0),
                     jnp.concatenate([other, packed], axis=0))
    partials = expert_part(both, gate_dev, up_dev, down_dev)
    mine = jnp.where(me == 0, partials[:capacity], partials[capacity:])
    theirs = jnp.where(me == 0, partials[capacity:], partials[:capacity])
    summed = mine.astype(jnp.float32) + swapped(theirs, "expert").astype(jnp.float32)
    share = jnp.dot(onehot.astype(jnp.float32), weight, precision=lax.Precision.HIGHEST)
    scaled = summed * share[:, None]
    h_rows = jnp.dot(onehot, current, preferred_element_type=jnp.float32)
    new_rows = (h_rows + scaled).astype(jnp.bfloat16)
    hole_slot = jnp.sum(jnp.where(pairs, slot[:bulk, None], 0), axis=0)
    tail_slot = jnp.where(kept[bulk:], slot[bulk:], jnp.where(tail_used, hole_slot, -1))
    carry = (tail_slot[:, None] == tail_iota[None, :]).astype(jnp.bfloat16)
    carried = jnp.dot(carry, new_rows, preferred_element_type=jnp.float32).astype(jnp.bfloat16)
    second = jnp.where((tail_slot >= 0)[:, None], carried, current[bulk:])
    second, mate = lax.optimization_barrier((second, jnp.concatenate([top_mate, tail_mate])))
    second = passed_along(second, "section", 1)
    mate = passed_along(mate, "section", 1)
    tail_mate = mate[bulk:]
    top_mate = jnp.where(row_iota < bulk, mate, -1)
    back_top = (top_mate[:, None] == tail_iota[None, :]).astype(jnp.bfloat16)
    out = jnp.where((top_mate >= 0)[:, None],
                    jnp.dot(back_top, second, preferred_element_type=jnp.float32).astype(jnp.bfloat16),
                    jnp.concatenate(moved_first + [second], axis=0))
    back_tail = (tail_mate[:, None] == row_iota[None, :bulk]).astype(jnp.bfloat16)
    raw_low = sum(jnp.dot(back_tail[:, a:b], part, preferred_element_type=jnp.float32)
                  for (a, b), part in zip(cuts, moved_first)).astype(jnp.bfloat16)
    raw_low = lax.optimization_barrier(raw_low)
    low = jnp.where((tail_mate >= 0)[:, None], raw_low, second)
    out = lax.dynamic_update_slice(out, low, (bulk, 0))
    return out[None]


def solution(mesh):
    return jax.shard_map(
        local,
        mesh=mesh,
        in_specs=(
            P("section", "expert", None),
            P("section", None),
            P("section", None, None),
            P("section", None, "expert"),
            P("section", None, "expert"),
            P("section", "expert", None),
            P(None, "section", "expert", None),
        ),
        out_specs=P("section", "expert", None),
        check_vma=False,
    )
```

```python
import jax
import jax.numpy as jnp
from jax import lax
from jax.sharding import PartitionSpec as P

LEAD_ROWS = 64


def passed_along(x, axis, by):
    devices = lax.axis_size(axis)
    return lax.ppermute(x, axis, [(i, (i + by) % devices) for i in range(devices)])


def swapped(x, axis):
    return lax.ppermute(x, axis, [(0, 1), (1, 0)])


def expert_part(piece, gate_dev, up_dev, down_dev):
    gate = jnp.dot(piece, gate_dev, preferred_element_type=jnp.float32)
    upper = jnp.dot(piece, up_dev, preferred_element_type=jnp.float32)
    active = (jax.nn.silu(gate) * upper).astype(jnp.bfloat16)
    partial_out = jnp.dot(active, down_dev, preferred_element_type=jnp.float32)
    return lax.optimization_barrier(partial_out.astype(jnp.bfloat16))


def local(state, norm_gain, router, w_gate, w_up, w_down, route_ids):
    gate_dev = w_gate[0]
    up_dev = w_up[0]
    down_dev = w_down[0]
    gain = norm_gain[0]
    table = router[0]
    current = state[0]
    rows = current.shape[0]
    capacity = rows // 8
    bulk = rows - capacity
    chosen = jnp.sum((route_ids[0, 0] == 0).astype(jnp.int32), axis=-1)
    row_iota = jnp.arange(rows, dtype=jnp.int32)
    before = (row_iota[None, :] < row_iota[:, None]).astype(jnp.bfloat16)

    def earlier(*cols):
        stack = jnp.stack(cols, axis=1).astype(jnp.bfloat16)
        sums = jnp.dot(before, stack, preferred_element_type=jnp.float32).astype(jnp.int32)
        return [sums[:, k] for k in range(len(cols))]

    (slot,) = earlier(chosen)
    kept = (chosen > 0) & (slot < capacity)
    hole = kept & (row_iota < bulk)
    free = jnp.logical_not(kept) & (row_iota >= bulk)
    hole_rank, free_rank = earlier(hole, free)
    n_holes = jnp.sum(hole.astype(jnp.int32))
    used = free & (free_rank < n_holes)
    top_hole, tail_used = hole[:bulk], used[bulk:]
    pairs = top_hole[:, None] & tail_used[None, :] & (hole_rank[:bulk, None] == free_rank[None, bulk:])
    tail_iota = jnp.arange(capacity, dtype=jnp.int32)
    top_mate = jnp.where(top_hole, jnp.sum(jnp.where(pairs, tail_iota[None, :], 0), axis=1), -1)
    tail_mate = jnp.where(tail_used, jnp.sum(jnp.where(pairs, row_iota[:bulk, None], 0), axis=0), -1)
    cuts = [(0, LEAD_ROWS), (LEAD_ROWS, bulk)]
    moved_first = []
    for a, b in cuts:
        fill = jnp.dot(pairs[a:b].astype(jnp.bfloat16), current[bulk:], preferred_element_type=jnp.float32)
        first = jnp.where(top_hole[a:b, None], fill.astype(jnp.bfloat16), current[a:b])
        moved_first.append(passed_along(first, "section", 1))
    me = lax.axis_index("expert")
    slot_iota = jnp.arange(capacity)[:, None]
    expert_iota = jnp.arange(table.shape[1])
    h32 = current.astype(jnp.float32)
    var = jnp.mean(h32 * h32, axis=-1, keepdims=True)
    normed = (h32 * lax.rsqrt(var + 1e-06) * gain).astype(jnp.bfloat16)
    scores = jax.nn.sigmoid(jnp.dot(normed, table, preferred_element_type=jnp.float32))
    ids = route_ids[0, 0]
    picked = jnp.sum((ids[:, :, None] == expert_iota[None, None, :]).astype(jnp.float32), axis=1)
    weight = 2.5 * scores[:, 0] * picked[:, 0] / jnp.sum(scores * picked, axis=-1)
    hit = kept[None, :] & (slot[None, :] == slot_iota)
    onehot = hit.astype(jnp.bfloat16)
    packed = jnp.dot(onehot, normed, preferred_element_type=jnp.float32).astype(jnp.bfloat16)
    other = swapped(packed, "expert")
    both = jnp.where(me == 0, jnp.concatenate([packed, other], axis=0),
                     jnp.concatenate([other, packed], axis=0))
    partials = expert_part(both, gate_dev, up_dev, down_dev)
    mine = jnp.where(me == 0, partials[:capacity], partials[capacity:])
    theirs = jnp.where(me == 0, partials[capacity:], partials[:capacity])
    summed = mine.astype(jnp.float32) + swapped(theirs, "expert").astype(jnp.float32)
    share = jnp.dot(onehot.astype(jnp.float32), weight, precision=lax.Precision.HIGHEST)
    scaled = summed * share[:, None]
    h_rows = jnp.dot(onehot, current, preferred_element_type=jnp.float32)
    new_rows = (h_rows + scaled).astype(jnp.bfloat16)
    hole_slot = jnp.sum(jnp.where(pairs, slot[:bulk, None], 0), axis=0)
    tail_slot = jnp.where(kept[bulk:], slot[bulk:], jnp.where(tail_used, hole_slot, -1))
    carry = (tail_slot[:, None] == tail_iota[None, :]).astype(jnp.bfloat16)
    carried = jnp.dot(carry, new_rows, preferred_element_type=jnp.float32).astype(jnp.bfloat16)
    second = jnp.where((tail_slot >= 0)[:, None], carried, current[bulk:])
    second, mate = lax.optimization_barrier((second, jnp.concatenate([top_mate, tail_mate])))
    second = passed_along(second, "section", 1)
    mate = passed_along(mate, "section", 1)
    tail_mate = mate[bulk:]

    def with_holes(a, b, part):
        ties = (mate[a:b, None] == tail_iota[None, :]).astype(jnp.bfloat16)
        filled = jnp.dot(ties, second, preferred_element_type=jnp.float32).astype(jnp.bfloat16)
        return jnp.where((mate[a:b] >= 0)[:, None], filled, part)

    (a0, b0), (a1, b1) = cuts
    out = jnp.pad(with_holes(a1, b1, moved_first[1]), ((a1, rows - b1), (0, 0)))
    out = lax.dynamic_update_slice(out, with_holes(a0, b0, moved_first[0]), (a0, 0))
    back_tail = (tail_mate[:, None] == row_iota[None, :bulk]).astype(jnp.bfloat16)
    raw_low = sum(jnp.dot(back_tail[:, a:b], part, preferred_element_type=jnp.float32)
                  for (a, b), part in zip(cuts, moved_first)).astype(jnp.bfloat16)
    raw_low = lax.optimization_barrier(raw_low)
    low = jnp.where((tail_mate >= 0)[:, None], raw_low, second)
    out = lax.dynamic_update_slice(out, low, (bulk, 0))
    return out[None]


def solution(mesh):
    return jax.shard_map(
        local,
        mesh=mesh,
        in_specs=(
            P("section", "expert", None),
            P("section", None),
            P("section", None, None),
            P("section", None, "expert"),
            P("section", None, "expert"),
            P("section", "expert", None),
            P(None, "section", "expert", None),
        ),
        out_specs=P("section", "expert", None),
        check_vma=False,
    )
```

```python
import jax
import jax.numpy as jnp
from jax import lax
from jax.sharding import PartitionSpec as P

LEAD_ROWS = 48


def passed_along(x, axis, by):
    devices = lax.axis_size(axis)
    return lax.ppermute(x, axis, [(i, (i + by) % devices) for i in range(devices)])


def swapped(x, axis):
    return lax.ppermute(x, axis, [(0, 1), (1, 0)])


def expert_part(piece, gate_dev, up_dev, down_dev):
    gate = jnp.dot(piece, gate_dev, preferred_element_type=jnp.float32)
    upper = jnp.dot(piece, up_dev, preferred_element_type=jnp.float32)
    active = (jax.nn.silu(gate) * upper).astype(jnp.bfloat16)
    partial_out = jnp.dot(active, down_dev, preferred_element_type=jnp.float32)
    return lax.optimization_barrier(partial_out.astype(jnp.bfloat16))


def local(state, norm_gain, router, w_gate, w_up, w_down, route_ids):
    gate_dev = w_gate[0]
    up_dev = w_up[0]
    down_dev = w_down[0]
    gain = norm_gain[0]
    table = router[0]
    current = state[0]
    rows = current.shape[0]
    capacity = rows // 8
    bulk = rows - capacity
    chosen = jnp.sum((route_ids[0, 0] == 0).astype(jnp.int32), axis=-1)
    row_iota = jnp.arange(rows, dtype=jnp.int32)
    before = (row_iota[None, :] < row_iota[:, None]).astype(jnp.bfloat16)

    def earlier(*cols):
        stack = jnp.stack(cols, axis=1).astype(jnp.bfloat16)
        sums = jnp.dot(before, stack, preferred_element_type=jnp.float32).astype(jnp.int32)
        return [sums[:, k] for k in range(len(cols))]

    (slot,) = earlier(chosen)
    kept = (chosen > 0) & (slot < capacity)
    hole = kept & (row_iota < bulk)
    free = jnp.logical_not(kept) & (row_iota >= bulk)
    hole_rank, free_rank = earlier(hole, free)
    n_holes = hole_rank[bulk]
    used = free & (free_rank < n_holes)
    top_hole, tail_used = hole[:bulk], used[bulk:]
    pairs = top_hole[:, None] & tail_used[None, :] & (hole_rank[:bulk, None] == free_rank[None, bulk:])
    tail_iota = jnp.arange(capacity, dtype=jnp.int32)
    top_mate = jnp.where(top_hole, jnp.sum(jnp.where(pairs, tail_iota[None, :], 0), axis=1), -1)
    tail_mate = jnp.where(tail_used, jnp.sum(jnp.where(pairs, row_iota[:bulk, None], 0), axis=0), -1)
    cuts = [(0, LEAD_ROWS), (LEAD_ROWS, bulk)]
    moved_first = []
    for a, b in cuts:
        fill = jnp.dot(pairs[a:b].astype(jnp.bfloat16), current[bulk:], preferred_element_type=jnp.float32)
        first = jnp.where(top_hole[a:b, None], fill.astype(jnp.bfloat16), current[a:b])
        moved_first.append(passed_along(first, "section", 1))
    me = lax.axis_index("expert")
    slot_iota = jnp.arange(capacity)[:, None]
    expert_iota = jnp.arange(table.shape[1])
    h32 = current.astype(jnp.float32)
    var = jnp.mean(h32 * h32, axis=-1, keepdims=True)
    normed = (h32 * lax.rsqrt(var + 1e-06) * gain).astype(jnp.bfloat16)
    scores = jax.nn.sigmoid(jnp.dot(normed, table, preferred_element_type=jnp.float32))
    ids = route_ids[0, 0]
    picked = jnp.sum((ids[:, :, None] == expert_iota[None, None, :]).astype(jnp.float32), axis=1)
    weight = 2.5 * scores[:, 0] * picked[:, 0] / jnp.sum(scores * picked, axis=-1)
    hit = kept[None, :] & (slot[None, :] == slot_iota)
    onehot = hit.astype(jnp.bfloat16)
    packed = jnp.dot(onehot, normed, preferred_element_type=jnp.float32).astype(jnp.bfloat16)
    other = swapped(packed, "expert")
    both = jnp.where(me == 0, jnp.concatenate([packed, other], axis=0),
                     jnp.concatenate([other, packed], axis=0))
    partials = expert_part(both, gate_dev, up_dev, down_dev)
    mine = jnp.where(me == 0, partials[:capacity], partials[capacity:])
    theirs = jnp.where(me == 0, partials[capacity:], partials[:capacity])
    summed = mine.astype(jnp.float32) + swapped(theirs, "expert").astype(jnp.float32)
    share = jnp.dot(onehot.astype(jnp.float32), weight, precision=lax.Precision.HIGHEST)
    scaled = summed * share[:, None]
    h_rows = jnp.dot(onehot, current, preferred_element_type=jnp.float32)
    new_rows = (h_rows + scaled).astype(jnp.bfloat16)
    hole_slot = jnp.sum(jnp.where(pairs, slot[:bulk, None], 0), axis=0)
    tail_slot = jnp.where(kept[bulk:], slot[bulk:], jnp.where(tail_used, hole_slot, -1))
    carry = (tail_slot[:, None] == tail_iota[None, :]).astype(jnp.bfloat16)
    carried = jnp.dot(carry, new_rows, preferred_element_type=jnp.float32).astype(jnp.bfloat16)
    second = jnp.where((tail_slot >= 0)[:, None], carried, current[bulk:])
    second, mate = lax.optimization_barrier((second, jnp.concatenate([top_mate, tail_mate])))
    second = passed_along(second, "section", 1)
    mate = passed_along(mate, "section", 1)
    tail_mate = mate[bulk:]
    back_tail = (tail_mate[:, None] == row_iota[None, :bulk]).astype(jnp.bfloat16)
    raw_low = sum(jnp.dot(back_tail[:, a:b], part, preferred_element_type=jnp.float32)
                  for (a, b), part in zip(cuts, moved_first)).astype(jnp.bfloat16)
    raw_low = lax.optimization_barrier(raw_low)
    low = jnp.where((tail_mate >= 0)[:, None], raw_low, second)
    top_mate = jnp.where(row_iota < bulk, mate, -1)
    back_top = (top_mate[:, None] == tail_iota[None, :]).astype(jnp.bfloat16)
    out = jnp.where((top_mate >= 0)[:, None],
                    jnp.dot(back_top, second, preferred_element_type=jnp.float32).astype(jnp.bfloat16),
                    jnp.concatenate(moved_first + [low], axis=0))
    return out[None]


def solution(mesh):
    return jax.shard_map(
        local,
        mesh=mesh,
        in_specs=(
            P("section", "expert", None),
            P("section", None),
            P("section", None, None),
            P("section", None, "expert"),
            P("section", None, "expert"),
            P("section", "expert", None),
            P(None, "section", "expert", None),
        ),
        out_specs=P("section", "expert", None),
        check_vma=False,
    )
```
